128 devices in a mesh: row: 16 (over z, y), col: 8 (over x, core).
Axes of the slice: x: 4, y: 4, z: 4, core: 2. Of those that a mesh axis runs over, the one named last changes fastest.
Arguments:
- queries: float32 [32768, 256], P(('row', 'col')), may hold values from -1 to 1
- passages: float32 [32768, 256], P(('col', 'row')), may hold values from -1 to 1
- mean_cost: float32 [1], replicated, may hold values from 1 to 3
Outputs:
- row_potential: float32 [32768], P('row')
- col_potential: float32 [32768], P('col')
The draws below stay inside these ranges and needn't reach their ends.
All inputs are finite; a program needn't handle non-finite values.
Results may differ from the reference program's by a relative error of at most 0.0003.
Values sent between devices are 32-bit elements; how exact they have to be, the bound alone decides.
No kernel may reach another device: no remote copies, remote signals or barrier semaphores. Data moves between devices by JAX's collectives and lax.ppermute only.
A program may use at most 256 MiB of HBM per device.

```python
import math
import jax
import jax.numpy as jnp
from jax import lax

D = 256
ITERS = 3
QUERIES = 32768
PASSAGES = 32768


def shared_pair(key):
    subkeys = [jax.random.fold_in(key, 101 + offset) for offset in range(6)]
    passage_base = jax.random.truncated_normal(subkeys[0], -4.0, 4.0, (PASSAGES, D), jnp.float32) * D ** (-0.5)
    query_base = jax.random.truncated_normal(subkeys[1], -4.0, 4.0, (QUERIES, D), jnp.float32) * D ** (-0.5)
    lower_log = math.log(0.5)
    upper_log = math.log(1.6)
    passage_scale = jnp.exp(jax.random.uniform(subkeys[2], (PASSAGES, 1), jnp.float32, lower_log, upper_log))
    query_scale = jnp.exp(jax.random.uniform(subkeys[3], (QUERIES, 1), jnp.float32, lower_log, upper_log))
    passages = passage_base * passage_scale
    queries = query_base * query_scale
    distant = query_base[8:16] + 6.0 * D ** (-0.5)
    queries = jnp.concatenate([queries[0:8], distant, queries[16:]], axis=0)
    return (queries, passages)


def draw_queries(key, part):
    return shared_pair(key)[0]


def draw_passages(key, part):
    return shared_pair(key)[1]


def setup_inputs(seed: int = 0) -> dict:
    splits = jax.random.split(jax.random.key(seed), 4)
    queries = draw_queries(jax.random.fold_in(splits[3], 71), 0)
    passages = draw_passages(jax.random.fold_in(splits[3], 71), 0)
    mean_cost = jnp.clip(jax.random.uniform(splits[2], (1,), jnp.float32, 1.0, 3.0), 1.0, 3.0)
    return dict(queries=queries, passages=passages, mean_cost=mean_cost)


def pair_costs(left, right):
    left_norms = jnp.sum(left * left, axis=1)
    right_norms = jnp.sum(right * right, axis=1)
    inner = jnp.dot(left, right.T, precision=lax.Precision.HIGHEST, preferred_element_type=jnp.float32)
    return (left_norms[:, None] + right_norms[None, :]) - 2.0 * inner


def block_logsum(left, right, potential, entropy_scale):
    width = math.gcd(left.shape[0], 512)
    blocks = left.reshape(left.shape[0] // width, width, left.shape[1])

    def one_block(block_rows):
        scores = (potential[None, :] - pair_costs(block_rows, right)) / entropy_scale
        peak = jnp.max(scores, axis=1)
        return peak + jnp.log(jnp.sum(jnp.exp(scores - peak[:, None]), axis=1))

    return lax.map(one_block, blocks).reshape(-1)


def reference(queries, passages, mean_cost):
    entropy_scale = 0.1 * mean_cost[0]
    col_potential = jnp.zeros((PASSAGES,), jnp.float32)
    row_potential = jnp.zeros((QUERIES,), jnp.float32)
    for repeat in range(ITERS):
        row_potential = -entropy_scale * math.log(QUERIES) - entropy_scale * block_logsum(queries, passages, col_potential, entropy_scale)
        col_potential = -entropy_scale * math.log(PASSAGES) - entropy_scale * block_logsum(passages, queries, row_potential, entropy_scale)
    return row_potential, col_potential
```

```python
import math

import jax
import jax.numpy as jnp
from jax import lax
from jax.sharding import PartitionSpec as P

ITERS = 3


def inner_costs(left, right):
    left_norms = jnp.sum(left * left, axis=1)
    right_norms = jnp.sum(right * right, axis=1)
    inner = lax.dot_general(
        left,
        right,
        (((1,), (1,)), ((), ())),
        precision=lax.Precision.HIGHEST,
        preferred_element_type=jnp.float32,
    )
    return left_norms[:, None] + right_norms[None, :] - 2.0 * inner


def combine_over(peak, total, axis):
    size = lax.axis_size(axis)
    packed = jnp.stack([peak, total])
    step = 1
    while step < size:
        perm = [(i, i ^ step) for i in range(size)]
        other = lax.ppermute(packed, axis, perm)
        new_peak = jnp.maximum(packed[0], other[0])
        new_total = packed[1] * jnp.exp(packed[0] - new_peak) + other[1] * jnp.exp(other[0] - new_peak)
        packed = jnp.stack([new_peak, new_total])
        step *= 2
    return packed[0] + jnp.log(packed[1])


def logsum_col(scores):
    peak = jnp.max(scores, axis=1)
    totals = jnp.sum(jnp.exp(scores - peak[:, None]), axis=1)
    return combine_over(peak, totals, "col")


def logsum_row(scores):
    peak = jnp.max(scores, axis=0)
    totals = jnp.sum(jnp.exp(scores - peak[None, :]), axis=0)
    return combine_over(peak, totals, "row")


def per_device(queries, passages, mean_cost):
    entropy_scale = 0.1 * mean_cost[0]
    row_count = lax.axis_size("row")
    col_count = lax.axis_size("col")
    all_queries = queries.shape[0] * row_count * col_count
    all_passages = passages.shape[0] * row_count * col_count
    query_block = lax.all_gather(queries, "col", axis=0, tiled=True)
    cost_tile = inner_costs(query_block, lax.all_gather(passages, "row", axis=0, tiled=True))
    col_potential = jnp.zeros((cost_tile.shape[1],), jnp.float32)
    row_potential = jnp.zeros((cost_tile.shape[0],), jnp.float32)
    for repeat in range(ITERS):
        scores = (col_potential[None, :] - cost_tile) / entropy_scale
        row_potential = -entropy_scale * math.log(all_queries) - entropy_scale * logsum_col(scores)
        scores = (row_potential[:, None] - cost_tile) / entropy_scale
        col_potential = -entropy_scale * math.log(all_passages) - entropy_scale * logsum_row(scores)
    return (row_potential, col_potential)


def solution(mesh):
    placed = (P(("row", "col"), None), P(("col", "row"), None), P())
    return jax.shard_map(
        per_device, mesh=mesh, in_specs=placed, out_specs=(P("row"), P("col")), check_vma=False
    )
```

```python
import math

import jax
import jax.numpy as jnp
from jax import lax
from jax.sharding import PartitionSpec as P

ITERS = 3


def inner_costs(left, right):
    left_norms = jnp.sum(left * left, axis=1)
    right_norms = jnp.sum(right * right, axis=1)
    inner = lax.dot_general(
        left,
        right,
        (((1,), (1,)), ((), ())),
        precision=lax.Precision.HIGHEST,
        preferred_element_type=jnp.float32,
    )
    return left_norms[:, None] + right_norms[None, :] - 2.0 * inner


def digit_partners(axis, size, stride, width, shift):
    perm = []
    for i in range(size):
        p = (i // stride) % width
        perm.append((i, i + (((p + shift) % width) - p) * stride))
    return perm


def exchange(x, axis, stride, width):
    size = lax.axis_size(axis)
    pos = (lax.axis_index(axis) // stride) % width
    received = [x] + [lax.ppermute(x, axis, digit_partners(axis, size, stride, width, k)) for k in range(1, width)]
    stacked = jnp.stack(received)
    return [lax.dynamic_index_in_dim(stacked, (pos - q) % width, 0, keepdims=False) for q in range(width)]


def combine_over(peak, total, axis, digits):
    packed = jnp.stack([peak, total])
    stride = 1
    for width in digits:
        parts = exchange(packed, axis, stride, width)
        new_peak = parts[0][0]
        for part in parts[1:]:
            new_peak = jnp.maximum(new_peak, part[0])
        new_total = parts[0][1] * jnp.exp(parts[0][0] - new_peak)
        for part in parts[1:]:
            new_total = new_total + part[1] * jnp.exp(part[0] - new_peak)
        packed = jnp.stack([new_peak, new_total])
        stride *= width
    return packed[0] + jnp.log(packed[1])


def radix_digits(size):
    digits = []
    while size > 1:
        width = 4 if size % 4 == 0 else 2
        digits.append(width)
        size //= width
    return tuple(digits)


def col_digits(size):
    if size % 2 == 0:
        return (2,) + radix_digits(size // 2)
    return radix_digits(size)


def logsum_col(scores):
    peak = jnp.max(scores, axis=1)
    totals = jnp.sum(jnp.exp(scores - peak[:, None]), axis=1)
    return combine_over(peak, totals, "col", col_digits(lax.axis_size("col")))


def logsum_row(scores):
    peak = jnp.max(scores, axis=0)
    totals = jnp.sum(jnp.exp(scores - peak[None, :]), axis=0)
    return combine_over(peak, totals, "row", radix_digits(lax.axis_size("row")))


def gather_col(x):
    size = lax.axis_size("col")
    return jnp.concatenate(exchange(x, "col", 1, size), axis=0)


def per_device(queries, passages, mean_cost):
    entropy_scale = 0.1 * mean_cost[0]
    row_count = lax.axis_size("row")
    col_count = lax.axis_size("col")
    all_queries = queries.shape[0] * row_count * col_count
    all_passages = passages.shape[0] * row_count * col_count
    query_block = gather_col(queries)
    cost_tile = inner_costs(query_block, lax.all_gather(passages, "row", axis=0, tiled=True))
    col_potential = jnp.zeros((cost_tile.shape[1],), jnp.float32)
    row_potential = jnp.zeros((cost_tile.shape[0],), jnp.float32)
    for repeat in range(ITERS):
        scores = (col_potential[None, :] - cost_tile) / entropy_scale
        row_potential = -entropy_scale * math.log(all_queries) - entropy_scale * logsum_col(scores)
        scores = (row_potential[:, None] - cost_tile) / entropy_scale
        col_potential = -entropy_scale * math.log(all_passages) - entropy_scale * logsum_row(scores)
    return (row_potential, col_potential)


def solution(mesh):
    placed = (P(("row", "col"), None), P(("col", "row"), None), P())
    return jax.shard_map(
        per_device, mesh=mesh, in_specs=placed, out_specs=(P("row"), P("col")), check_vma=False
    )
```

```python
import math

import jax
import jax.numpy as jnp
from jax import lax
from jax.sharding import PartitionSpec as P

ITERS = 3


def inner_costs(left, right):
    left_norms = jnp.sum(left * left, axis=1)
    right_norms = jnp.sum(right * right, axis=1)
    inner = lax.dot_general(
        left,
        right,
        (((1,), (1,)), ((), ())),
        precision=lax.Precision.HIGHEST,
        preferred_element_type=jnp.float32,
    )
    return left_norms[:, None] + right_norms[None, :] - 2.0 * inner


def digit_partners(axis, size, stride, width, shift):
    perm = []
    for i in range(size):
        p = (i // stride) % width
        perm.append((i, i + (((p + shift) % width) - p) * stride))
    return perm


def exchange(x, axis, stride, width):
    size = lax.axis_size(axis)
    pos = (lax.axis_index(axis) // stride) % width
    received = [x] + [lax.ppermute(x, axis, digit_partners(axis, size, stride, width, k)) for k in range(1, width)]
    stacked = jnp.stack(received)
    return [lax.dynamic_index_in_dim(stacked, (pos - q) % width, 0, keepdims=False) for q in range(width)]


def combine_over(peak, total, axis, digits):
    packed = jnp.stack([peak, total])
    stride = 1
    for width in digits:
        parts = exchange(packed, axis, stride, width)
        new_peak = parts[0][0]
        for part in parts[1:]:
            new_peak = jnp.maximum(new_peak, part[0])
        new_total = parts[0][1] * jnp.exp(parts[0][0] - new_peak)
        for part in parts[1:]:
            new_total = new_total + part[1] * jnp.exp(part[0] - new_peak)
        packed = jnp.stack([new_peak, new_total])
        stride *= width
    return packed[0] + jnp.log(packed[1])


def radix_digits(size):
    digits = []
    while size > 1:
        width = 4 if size % 4 == 0 else 2
        digits.append(width)
        size //= width
    return tuple(digits)


def col_digits(size):
    if size % 2 == 0:
        return (2,) + radix_digits(size // 2)
    return radix_digits(size)


def logsum_col(scores):
    peak = jnp.max(scores, axis=1)
    totals = jnp.sum(jnp.exp(scores - peak[:, None]), axis=1)
    return combine_over(peak, totals, "col", col_digits(lax.axis_size("col")))


def logsum_row(scores):
    peak = jnp.max(scores, axis=0)
    totals = jnp.sum(jnp.exp(scores - peak[None, :]), axis=0)
    return combine_over(peak, totals, "row", radix_digits(lax.axis_size("row")))


def gather_col(x):
    size = lax.axis_size("col")
    return jnp.concatenate(exchange(x, "col", 1, size), axis=0)


def per_device(queries, passages, mean_cost):
    entropy_scale = 0.1 * mean_cost[0]
    row_count = lax.axis_size("row")
    col_count = lax.axis_size("col")
    all_queries = queries.shape[0] * row_count * col_count
    all_passages = passages.shape[0] * row_count * col_count
    query_block = gather_col(queries)
    cost_tile = inner_costs(query_block, lax.all_gather(passages, "row", axis=0, tiled=True))
    col_potential = jnp.zeros((cost_tile.shape[1],), jnp.float32)
    row_potential = jnp.zeros((cost_tile.shape[0],), jnp.float32)

    def one_iteration(repeat, potentials):
        row_potential, col_potential = potentials
        scores = (col_potential[None, :] - cost_tile) / entropy_scale
        row_potential = -entropy_scale * math.log(all_queries) - entropy_scale * logsum_col(scores)
        scores = (row_potential[:, None] - cost_tile) / entropy_scale
        col_potential = -entropy_scale * math.log(all_passages) - entropy_scale * logsum_row(scores)
        return (row_potential, col_potential)

    return lax.fori_loop(0, ITERS, one_iteration, (row_potential, col_potential))


def solution(mesh):
    placed = (P(("row", "col"), None), P(("col", "row"), None), P())
    return jax.shard_map(
        per_device, mesh=mesh, in_specs=placed, out_specs=(P("row"), P("col")), check_vma=False
    )
```

```python
import math

import jax
import jax.numpy as jnp
from jax import lax
from jax.experimental import pallas as pl
from jax.experimental.pallas import tpu as pltpu
from jax.sharding import PartitionSpec as P

ITERS = 3


def inner_costs(left, right):
    left_norms = jnp.sum(left * left, axis=1)
    right_norms = jnp.sum(right * right, axis=1)
    inner = lax.dot_general(
        left,
        right,
        (((1,), (1,)), ((), ())),
        precision=lax.Precision.HIGHEST,
        preferred_element_type=jnp.float32,
    )
    return left_norms[:, None] + right_norms[None, :] - 2.0 * inner


def digit_partners(axis, size, stride, width, shift):
    perm = []
    for i in range(size):
        p = (i // stride) % width
        perm.append((i, i + (((p + shift) % width) - p) * stride))
    return perm


def exchange(x, axis, stride, width):
    size = lax.axis_size(axis)
    pos = (lax.axis_index(axis) // stride) % width
    received = [x] + [lax.ppermute(x, axis, digit_partners(axis, size, stride, width, k)) for k in range(1, width)]
    stacked = jnp.stack(received)
    return [lax.dynamic_index_in_dim(stacked, (pos - q) % width, 0, keepdims=False) for q in range(width)]


def combine_over(peak, total, axis, digits):
    packed = jnp.stack([peak, total])
    stride = 1
    for width in digits:
        parts = exchange(packed, axis, stride, width)
        new_peak = parts[0][0]
        for part in parts[1:]:
            new_peak = jnp.maximum(new_peak, part[0])
        new_total = parts[0][1] * jnp.exp(parts[0][0] - new_peak)
        for part in parts[1:]:
            new_total = new_total + part[1] * jnp.exp(part[0] - new_peak)
        packed = jnp.stack([new_peak, new_total])
        stride *= width
    return packed[0] + jnp.log(packed[1])


def radix_digits(size):
    digits = []
    while size > 1:
        width = 4 if size % 4 == 0 else 2
        digits.append(width)
        size //= width
    return tuple(digits)


def col_digits(size):
    if size % 2 == 0:
        return (2,) + radix_digits(size // 2)
    return radix_digits(size)


def row_block_kernel(scale_ref, potential_ref, cost_ref, peak_ref, total_ref):
    scores = (potential_ref[...] - cost_ref[...]) / scale_ref[...]
    peak = jnp.max(scores, axis=1, keepdims=True)
    peak_ref[...] = peak
    total_ref[...] = jnp.sum(jnp.exp(scores - peak), axis=1, keepdims=True)


def col_block_kernel(scale_ref, potential_ref, cost_ref, peak_ref, total_ref):
    scores = (potential_ref[...] - cost_ref[...]) / scale_ref[...]
    peak = jnp.max(scores, axis=0, keepdims=True)
    peak_ref[...] = peak
    total_ref[...] = jnp.sum(jnp.exp(scores - peak), axis=0, keepdims=True)


def local_logsum_rows(cost_tile, col_potential, scale, rows=256):
    m, n = cost_tile.shape
    est = pl.CostEstimate(flops=5 * m * n, transcendentals=m * n, bytes_accessed=4 * (m * n + n + 2 * m))
    peak, total = pl.pallas_call(
        row_block_kernel,
        grid=(m // rows,),
        in_specs=[
            pl.BlockSpec((1, 1), lambda i: (0, 0)),
            pl.BlockSpec((1, n), lambda i: (0, 0)),
            pl.BlockSpec((rows, n), lambda i: (i, 0)),
        ],
        out_specs=[pl.BlockSpec((rows, 1), lambda i: (i, 0)), pl.BlockSpec((rows, 1), lambda i: (i, 0))],
        out_shape=[jax.ShapeDtypeStruct((m, 1), jnp.float32)] * 2,
        cost_estimate=est,
    )(scale.reshape(1, 1), col_potential.reshape(1, n), cost_tile)
    return peak.reshape(m), total.reshape(m)


def local_logsum_cols(cost_tile, row_potential, scale, cols=512):
    m, n = cost_tile.shape
    est = pl.CostEstimate(flops=5 * m * n, transcendentals=m * n, bytes_accessed=4 * (m * n + m + 2 * n))
    peak, total = pl.pallas_call(
        col_block_kernel,
        grid=(n // cols,),
        in_specs=[
            pl.BlockSpec((1, 1), lambda j: (0, 0)),
            pl.BlockSpec((m, 1), lambda j: (0, 0)),
            pl.BlockSpec((m, cols), lambda j: (0, j)),
        ],
        out_specs=[pl.BlockSpec((1, cols), lambda j: (0, j)), pl.BlockSpec((1, cols), lambda j: (0, j))],
        out_shape=[jax.ShapeDtypeStruct((1, n), jnp.float32)] * 2,
        cost_estimate=est,
    )(scale.reshape(1, 1), row_potential.reshape(m, 1), cost_tile)
    return peak.reshape(n), total.reshape(n)


def gather_col(x):
    size = lax.axis_size("col")
    return jnp.concatenate(exchange(x, "col", 1, size), axis=0)


def per_device(queries, passages, mean_cost):
    entropy_scale = 0.1 * mean_cost[0]
    row_count = lax.axis_size("row")
    col_count = lax.axis_size("col")
    all_queries = queries.shape[0] * row_count * col_count
    all_passages = passages.shape[0] * row_count * col_count
    query_block = gather_col(queries)
    cost_tile = inner_costs(query_block, lax.all_gather(passages, "row", axis=0, tiled=True))
    col_potential = jnp.zeros((cost_tile.shape[1],), jnp.float32)
    row_potential = jnp.zeros((cost_tile.shape[0],), jnp.float32)
    for repeat in range(ITERS):
        peak, total = local_logsum_rows(cost_tile, col_potential, entropy_scale)
        logsum = combine_over(peak, total, "col", col_digits(col_count))
        row_potential = -entropy_scale * math.log(all_queries) - entropy_scale * logsum
        peak, total = local_logsum_cols(cost_tile, row_potential, entropy_scale)
        logsum = combine_over(peak, total, "row", radix_digits(row_count))
        col_potential = -entropy_scale * math.log(all_passages) - entropy_scale * logsum
    return (row_potential, col_potential)


def solution(mesh):
    placed = (P(("row", "col"), None), P(("col", "row"), None), P())
    return jax.shard_map(
        per_device, mesh=mesh, in_specs=placed, out_specs=(P("row"), P("col")), check_vma=False
    )
```

```python
import math

import jax
import jax.numpy as jnp
from jax import lax
from jax.sharding import PartitionSpec as P

ITERS = 3


def inner_costs(left, right):
    left_norms = jnp.sum(left * left, axis=1)
    right_norms = jnp.sum(right * right, axis=1)
    inner = lax.dot_general(
        left,
        right,
        (((1,), (1,)), ((), ())),
        precision=lax.Precision.HIGHEST,
        preferred_element_type=jnp.float32,
    )
    return left_norms[:, None] + right_norms[None, :] - 2.0 * inner


def digit_partners(axis, size, stride, width, shift):
    perm = []
    for i in range(size):
        p = (i // stride) % width
        perm.append((i, i + (((p + shift) % width) - p) * stride))
    return perm


def exchange(x, axis, stride, width):
    size = lax.axis_size(axis)
    pos = (lax.axis_index(axis) // stride) % width
    received = [x] + [lax.ppermute(x, axis, digit_partners(axis, size, stride, width, k)) for k in range(1, width)]
    stacked = jnp.stack(received)
    return [lax.dynamic_index_in_dim(stacked, (pos - q) % width, 0, keepdims=False) for q in range(width)]


def combine_over(peak, total, axis, digits):
    packed = jnp.stack([peak, total])
    stride = 1
    for width in digits:
        parts = exchange(packed, axis, stride, width)
        new_peak = parts[0][0]
        for part in parts[1:]:
            new_peak = jnp.maximum(new_peak, part[0])
        new_total = parts[0][1] * jnp.exp(parts[0][0] - new_peak)
        for part in parts[1:]:
            new_total = new_total + part[1] * jnp.exp(part[0] - new_peak)
        packed = jnp.stack([new_peak, new_total])
        stride *= width
    return packed[0] + jnp.log(packed[1])


def radix_digits(size):
    digits = []
    while size > 1:
        width = 4 if size % 4 == 0 else 2
        digits.append(width)
        size //= width
    return tuple(digits)


def col_digits(size):
    if size % 2 == 0:
        return (2,) + radix_digits(size // 2)
    return radix_digits(size)


def merge_pairs(first, second):
    peak = jnp.maximum(first[0], second[0])
    total = first[1] * jnp.exp(first[0] - peak) + second[1] * jnp.exp(second[0] - peak)
    return peak, total


def partial_rows(cost_block, col_potential, scale):
    scores = (col_potential[None, :] - cost_block) / scale
    peak = jnp.max(scores, axis=1)
    return peak, jnp.sum(jnp.exp(scores - peak[:, None]), axis=1)


def partial_cols(cost_block, row_potential, scale):
    scores = (row_potential[:, None] - cost_block) / scale
    peak = jnp.max(scores, axis=0)
    return peak, jnp.sum(jnp.exp(scores - peak[None, :]), axis=0)


def gather_col(x):
    size = lax.axis_size("col")
    return jnp.concatenate(exchange(x, "col", 1, size), axis=0)


def per_device(queries, passages, mean_cost):
    entropy_scale = 0.1 * mean_cost[0]
    row_count = lax.axis_size("row")
    col_count = lax.axis_size("col")
    all_queries = queries.shape[0] * row_count * col_count
    all_passages = passages.shape[0] * row_count * col_count
    query_block = gather_col(queries)
    passage_block = lax.all_gather(passages, "row", axis=0, tiled=True)
    q_halves = jnp.split(query_block, 2, axis=0)
    p_halves = jnp.split(passage_block, 2, axis=0)
    blocks = [[inner_costs(q, p) for p in p_halves] for q in q_halves]
    col_digit_list = col_digits(col_count)
    row_digit_list = radix_digits(row_count)
    col_potential = [jnp.zeros((p.shape[0],), jnp.float32) for p in p_halves]
    row_potential = [jnp.zeros((q.shape[0],), jnp.float32) for q in q_halves]
    for repeat in range(ITERS):
        for a in range(2):
            pair = merge_pairs(
                partial_rows(blocks[a][0], col_potential[0], entropy_scale),
                partial_rows(blocks[a][1], col_potential[1], entropy_scale),
            )
            logsum = combine_over(pair[0], pair[1], "col", col_digit_list)
            row_potential[a] = -entropy_scale * math.log(all_queries) - entropy_scale * logsum
        for b in range(2):
            pair = merge_pairs(
                partial_cols(blocks[0][b], row_potential[0], entropy_scale),
                partial_cols(blocks[1][b], row_potential[1], entropy_scale),
            )
            logsum = combine_over(pair[0], pair[1], "row", row_digit_list)
            col_potential[b] = -entropy_scale * math.log(all_passages) - entropy_scale * logsum
    return (jnp.concatenate(row_potential), jnp.concatenate(col_potential))


def solution(mesh):
    placed = (P(("row", "col"), None), P(("col", "row"), None), P())
    return jax.shard_map(
        per_device, mesh=mesh, in_specs=placed, out_specs=(P("row"), P("col")), check_vma=False
    )
```

```python
import math

import jax
import jax.numpy as jnp
from jax import lax
from jax.sharding import PartitionSpec as P

ITERS = 3


def inner_costs(left, right):
    left_norms = jnp.sum(left * left, axis=1)
    right_norms = jnp.sum(right * right, axis=1)
    inner = lax.dot_general(
        left,
        right,
        (((1,), (1,)), ((), ())),
        precision=lax.Precision.HIGHEST,
        preferred_element_type=jnp.float32,
    )
    return left_norms[:, None] + right_norms[None, :] - 2.0 * inner


def digit_partners(axis, size, stride, width, shift):
    perm = []
    for i in range(size):
        p = (i // stride) % width
        perm.append((i, i + (((p + shift) % width) - p) * stride))
    return perm


def exchange(x, axis, stride, width):
    size = lax.axis_size(axis)
    pos = (lax.axis_index(axis) // stride) % width
    received = [x] + [lax.ppermute(x, axis, digit_partners(axis, size, stride, width, k)) for k in range(1, width)]
    stacked = jnp.stack(received)
    return [lax.dynamic_index_in_dim(stacked, (pos - q) % width, 0, keepdims=False) for q in range(width)]


def combine_over(peak, total, axis, digits):
    size = lax.axis_size(axis)
    packed = jnp.stack([peak, total])
    stride = 1
    for width in digits:
        parts = [packed] + [
            lax.ppermute(packed, axis, digit_partners(axis, size, stride, width, k)) for k in range(1, width)
        ]
        new_peak = parts[0][0]
        for part in parts[1:]:
            new_peak = jnp.maximum(new_peak, part[0])
        terms = [part[1] * jnp.exp(part[0] - new_peak) for part in parts]
        if width == 4:
            new_total = (terms[0] + terms[2]) + (terms[1] + terms[3])
        else:
            new_total = terms[0] + terms[1]
        packed = jnp.stack([new_peak, new_total])
        stride *= width
    return packed[0] + jnp.log(packed[1])


def radix_digits(size):
    digits = []
    while size > 1:
        width = 4 if size % 4 == 0 else 2
        digits.append(width)
        size //= width
    return tuple(digits)


def col_digits(size):
    if size % 2 == 0:
        return (2,) + radix_digits(size // 2)
    return radix_digits(size)


def logsum_col(scores):
    peak = jnp.max(scores, axis=1)
    totals = jnp.sum(jnp.exp(scores - peak[:, None]), axis=1)
    return combine_over(peak, totals, "col", col_digits(lax.axis_size("col")))


def logsum_row(scores):
    peak = jnp.max(scores, axis=0)
    totals = jnp.sum(jnp.exp(scores - peak[None, :]), axis=0)
    return combine_over(peak, totals, "row", radix_digits(lax.axis_size("row")))


def gather_col(x):
    size = lax.axis_size("col")
    return jnp.concatenate(exchange(x, "col", 1, size), axis=0)


def per_device(queries, passages, mean_cost):
    entropy_scale = 0.1 * mean_cost[0]
    row_count = lax.axis_size("row")
    col_count = lax.axis_size("col")
    all_queries = queries.shape[0] * row_count * col_count
    all_passages = passages.shape[0] * row_count * col_count
    query_block = gather_col(queries)
    cost_tile = inner_costs(query_block, lax.all_gather(passages, "row", axis=0, tiled=True))
    col_potential = jnp.zeros((cost_tile.shape[1],), jnp.float32)
    row_potential = jnp.zeros((cost_tile.shape[0],), jnp.float32)
    for repeat in range(ITERS):
        scores = (col_potential[None, :] - cost_tile) / entropy_scale
        row_potential = -entropy_scale * math.log(all_queries) - entropy_scale * logsum_col(scores)
        scores = (row_potential[:, None] - cost_tile) / entropy_scale
        col_potential = -entropy_scale * math.log(all_passages) - entropy_scale * logsum_row(scores)
    return (row_potential, col_potential)


def solution(mesh):
    placed = (P(("row", "col"), None), P(("col", "row"), None), P())
    return jax.shard_map(
        per_device, mesh=mesh, in_specs=placed, out_specs=(P("row"), P("col")), check_vma=False
    )
```

```python
import math

import jax
import jax.numpy as jnp
from jax import lax
from jax.sharding import PartitionSpec as P

ITERS = 3


def inner_costs(left, right):
    left_norms = jnp.sum(left * left, axis=1)
    right_norms = jnp.sum(right * right, axis=1)
    inner = lax.dot_general(
        left,
        right,
        (((1,), (1,)), ((), ())),
        precision=lax.Precision.HIGHEST,
        preferred_element_type=jnp.float32,
    )
    return left_norms[:, None] + right_norms[None, :] - 2.0 * inner


def digit_partners(axis, size, stride, width, shift):
    perm = []
    for i in range(size):
        p = (i // stride) % width
        perm.append((i, i + (((p + shift) % width) - p) * stride))
    return perm


def exchange(x, axis, stride, width):
    size = lax.axis_size(axis)
    pos = (lax.axis_index(axis) // stride) % width
    received = [x] + [lax.ppermute(x, axis, digit_partners(axis, size, stride, width, k)) for k in range(1, width)]
    stacked = jnp.stack(received)
    return [lax.dynamic_index_in_dim(stacked, (pos - q) % width, 0, keepdims=False) for q in range(width)]


def combine_over(peak, total, axis, digits):
    size = lax.axis_size(axis)
    packed = jnp.stack([peak, total])
    stride = 1
    for width in digits:
        parts = [packed] + [
            lax.ppermute(packed, axis, digit_partners(axis, size, stride, width, k)) for k in range(1, width)
        ]
        new_peak = parts[0][0]
        for part in parts[1:]:
            new_peak = jnp.maximum(new_peak, part[0])
        terms = [part[1] * jnp.exp(part[0] - new_peak) for part in parts]
        if width == 4:
            new_total = (terms[0] + terms[2]) + (terms[1] + terms[3])
        else:
            new_total = terms[0] + terms[1]
        packed = jnp.stack([new_peak, new_total])
        stride *= width
    return packed[0] + jnp.log(packed[1])


def radix_digits(size):
    digits = []
    while size > 1:
        width = 4 if size % 4 == 0 else 2
        digits.append(width)
        size //= width
    return tuple(digits)


def col_digits(size):
    if size % 2 == 0:
        return (2,) + radix_digits(size // 2)
    return radix_digits(size)


def logsum_col(scores):
    peak = jnp.max(scores, axis=1)
    totals = jnp.sum(jnp.exp(scores - peak[:, None]), axis=1)
    return combine_over(peak, totals, "col", col_digits(lax.axis_size("col")))


def logsum_row(scores):
    peak = jnp.max(scores, axis=0)
    totals = jnp.sum(jnp.exp(scores - peak[None, :]), axis=0)
    return combine_over(peak, totals, "row", radix_digits(lax.axis_size("row")))


def gather_col(x):
    size = lax.axis_size("col")
    return jnp.concatenate(exchange(x, "col", 1, size), axis=0)


def gather_row(x):
    stride = 1
    for width in radix_digits(lax.axis_size("row")):
        x = jnp.concatenate(exchange(x, "row", stride, width), axis=0)
        stride *= width
    return x


def per_device(queries, passages, mean_cost):
    entropy_scale = 0.1 * mean_cost[0]
    row_count = lax.axis_size("row")
    col_count = lax.axis_size("col")
    all_queries = queries.shape[0] * row_count * col_count
    all_passages = passages.shape[0] * row_count * col_count
    query_block = gather_col(queries)
    cost_tile = inner_costs(query_block, gather_row(passages))
    col_potential = jnp.zeros((cost_tile.shape[1],), jnp.float32)
    row_potential = jnp.zeros((cost_tile.shape[0],), jnp.float32)
    for repeat in range(ITERS):
        scores = (col_potential[None, :] - cost_tile) / entropy_scale
        row_potential = -entropy_scale * math.log(all_queries) - entropy_scale * logsum_col(scores)
        scores = (row_potential[:, None] - cost_tile) / entropy_scale
        col_potential = -entropy_scale * math.log(all_passages) - entropy_scale * logsum_row(scores)
    return (row_potential, col_potential)


def solution(mesh):
    placed = (P(("row", "col"), None), P(("col", "row"), None), P())
    return jax.shard_map(
        per_device, mesh=mesh, in_specs=placed, out_specs=(P("row"), P("col")), check_vma=False
    )
```

```python
import math

import jax
import jax.numpy as jnp
from jax import lax
from jax.sharding import PartitionSpec as P

ITERS = 3


def inner_costs(left, right):
    left_norms = jnp.sum(left * left, axis=1)
    right_norms = jnp.sum(right * right, axis=1)
    inner = lax.dot_general(
        left,
        right,
        (((1,), (1,)), ((), ())),
        precision=lax.Precision.HIGHEST,
        preferred_element_type=jnp.float32,
    )
    return left_norms[:, None] + right_norms[None, :] - 2.0 * inner


def digit_partners(axis, size, stride, width, shift):
    perm = []
    for i in range(size):
        p = (i // stride) % width
        perm.append((i, i + (((p + shift) % width) - p) * stride))
    return perm


def exchange(x, axis, stride, width):
    size = lax.axis_size(axis)
    pos = (lax.axis_index(axis) // stride) % width
    received = [x] + [lax.ppermute(x, axis, digit_partners(axis, size, stride, width, k)) for k in range(1, width)]
    stacked = jnp.stack(received)
    return [lax.dynamic_index_in_dim(stacked, (pos - q) % width, 0, keepdims=False) for q in range(width)]


def combine_over(peak, total, axis, digits):
    size = lax.axis_size(axis)
    packed = jnp.stack([peak, total])
    stride = 1
    for width in digits:
        parts = [packed] + [
            lax.ppermute(packed, axis, digit_partners(axis, size, stride, width, k)) for k in range(1, width)
        ]
        new_peak = parts[0][0]
        for part in parts[1:]:
            new_peak = jnp.maximum(new_peak, part[0])
        terms = [part[1] * jnp.exp(part[0] - new_peak) for part in parts]
        if width == 4:
            new_total = (terms[0] + terms[2]) + (terms[1] + terms[3])
        else:
            new_total = terms[0] + terms[1]
        packed = jnp.stack([new_peak, new_total])
        stride *= width
    return packed[0] + jnp.log(packed[1])


def radix_digits(size):
    digits = []
    while size > 1:
        width = 4 if size % 4 == 0 else 2
        digits.append(width)
        size //= width
    return tuple(digits)


def col_digits(size):
    if size % 2 == 0:
        return (2,) + radix_digits(size // 2)
    return radix_digits(size)


def logsum_col(gaps, scale):
    peak = jnp.max(gaps, axis=1) / scale
    totals = jnp.sum(jnp.exp(gaps / scale - peak[:, None]), axis=1)
    return combine_over(peak, totals, "col", col_digits(lax.axis_size("col")))


def logsum_row(gaps, scale):
    peak = jnp.max(gaps, axis=0) / scale
    totals = jnp.sum(jnp.exp(gaps / scale - peak[None, :]), axis=0)
    return combine_over(peak, totals, "row", radix_digits(lax.axis_size("row")))


def gather_col(x):
    size = lax.axis_size("col")
    return jnp.concatenate(exchange(x, "col", 1, size), axis=0)


def per_device(queries, passages, mean_cost):
    entropy_scale = 0.1 * mean_cost[0]
    row_count = lax.axis_size("row")
    col_count = lax.axis_size("col")
    all_queries = queries.shape[0] * row_count * col_count
    all_passages = passages.shape[0] * row_count * col_count
    query_block = gather_col(queries)
    cost_tile = inner_costs(query_block, lax.all_gather(passages, "row", axis=0, tiled=True))
    col_potential = jnp.zeros((cost_tile.shape[1],), jnp.float32)
    row_potential = jnp.zeros((cost_tile.shape[0],), jnp.float32)
    for repeat in range(ITERS):
        gaps = col_potential[None, :] - cost_tile
        row_potential = -entropy_scale * math.log(all_queries) - entropy_scale * logsum_col(gaps, entropy_scale)
        gaps = row_potential[:, None] - cost_tile
        col_potential = -entropy_scale * math.log(all_passages) - entropy_scale * logsum_row(gaps, entropy_scale)
    return (row_potential, col_potential)


def solution(mesh):
    placed = (P(("row", "col"), None), P(("col", "row"), None), P())
    return jax.shard_map(
        per_device, mesh=mesh, in_specs=placed, out_specs=(P("row"), P("col")), check_vma=False
    )
```

```python
import math

import jax
import jax.numpy as jnp
from jax import lax
from jax.sharding import PartitionSpec as P

ITERS = 3


def inner_costs(left, right):
    left_norms = jnp.sum(left * left, axis=1)
    right_norms = jnp.sum(right * right, axis=1)
    inner = lax.dot_general(
        left,
        right,
        (((1,), (1,)), ((), ())),
        precision=lax.Precision.HIGHEST,
        preferred_element_type=jnp.float32,
    )
    return left_norms[:, None] + right_norms[None, :] - 2.0 * inner


def digit_partners(axis, size, stride, width, shift):
    perm = []
    for i in range(size):
        p = (i // stride) % width
        perm.append((i, i + (((p + shift) % width) - p) * stride))
    return perm


def exchange(x, axis, stride, width):
    size = lax.axis_size(axis)
    pos = (lax.axis_index(axis) // stride) % width
    received = [x] + [lax.ppermute(x, axis, digit_partners(axis, size, stride, width, k)) for k in range(1, width)]
    stacked = jnp.stack(received)
    return [lax.dynamic_index_in_dim(stacked, (pos - q) % width, 0, keepdims=False) for q in range(width)]


def combine_over(peak, total, axis, digits):
    size = lax.axis_size(axis)
    packed = jnp.stack([peak, total])
    stride = 1
    for width in digits:
        parts = [packed] + [
            lax.ppermute(packed, axis, digit_partners(axis, size, stride, width, k)) for k in range(1, width)
        ]
        new_peak = parts[0][0]
        for part in parts[1:]:
            new_peak = jnp.maximum(new_peak, part[0])
        terms = [part[1] * jnp.exp(part[0] - new_peak) for part in parts]
        if width == 4:
            new_total = (terms[0] + terms[2]) + (terms[1] + terms[3])
        else:
            new_total = terms[0] + terms[1]
        packed = jnp.stack([new_peak, new_total])
        stride *= width
    return packed[0] + jnp.log(packed[1])


def radix_digits(size):
    digits = []
    while size > 1:
        width = 4 if size % 4 == 0 else 2
        digits.append(width)
        size //= width
    return tuple(digits)


def col_digits(size):
    if size % 2 == 0:
        return (2,) + radix_digits(size // 2)
    return radix_digits(size)


def logsum_col(gaps, scale):
    peak = jnp.max(gaps, axis=1) / scale
    totals = jnp.sum(jnp.exp(gaps / scale - peak[:, None]), axis=1)
    return combine_over(peak, totals, "col", col_digits(lax.axis_size("col")))


def logsum_row(gaps, scale):
    peak = jnp.max(gaps, axis=0) / scale
    totals = jnp.sum(jnp.exp(gaps / scale - peak[None, :]), axis=0)
    return combine_over(peak, totals, "row", radix_digits(lax.axis_size("row")))


def gather_col(x):
    size = lax.axis_size("col")
    return jnp.concatenate(exchange(x, "col", 1, size), axis=0)


def per_device(queries, passages, mean_cost):
    entropy_scale = 0.1 * mean_cost[0]
    row_count = lax.axis_size("row")
    col_count = lax.axis_size("col")
    all_queries = queries.shape[0] * row_count * col_count
    all_passages = passages.shape[0] * row_count * col_count
    query_block = gather_col(queries)
    passage_block = lax.all_gather(passages, "row", axis=0, tiled=True)
    cost_tile = jnp.concatenate([inner_costs(chunk, passage_block) for chunk in jnp.split(query_block, 8, axis=0)], axis=0)
    col_potential = jnp.zeros((cost_tile.shape[1],), jnp.float32)
    row_potential = jnp.zeros((cost_tile.shape[0],), jnp.float32)
    for repeat in range(ITERS):
        gaps = col_potential[None, :] - cost_tile
        row_potential = -entropy_scale * math.log(all_queries) - entropy_scale * logsum_col(gaps, entropy_scale)
        gaps = row_potential[:, None] - cost_tile
        col_potential = -entropy_scale * math.log(all_passages) - entropy_scale * logsum_row(gaps, entropy_scale)
    return (row_potential, col_potential)


def solution(mesh):
    placed = (P(("row", "col"), None), P(("col", "row"), None), P())
    return jax.shard_map(
        per_device, mesh=mesh, in_specs=placed, out_specs=(P("row"), P("col")), check_vma=False
    )
```

```python
import math

import jax
import jax.numpy as jnp
from jax import lax
from jax.sharding import PartitionSpec as P

ITERS = 3


def inner_costs(left, right):
    left_norms = jnp.sum(left * left, axis=1)
    right_norms = jnp.sum(right * right, axis=1)
    inner = lax.dot_general(
        left,
        right,
        (((1,), (1,)), ((), ())),
        precision=lax.Precision.HIGHEST,
        preferred_element_type=jnp.float32,
    )
    return left_norms[:, None] + right_norms[None, :] - 2.0 * inner


def digit_partners(axis, size, stride, width, shift):
    perm = []
    for i in range(size):
        p = (i // stride) % width
        perm.append((i, i + (((p + shift) % width) - p) * stride))
    return perm


def exchange(x, axis, stride, width):
    size = lax.axis_size(axis)
    pos = (lax.axis_index(axis) // stride) % width
    received = [x] + [lax.ppermute(x, axis, digit_partners(axis, size, stride, width, k)) for k in range(1, width)]
    stacked = jnp.stack(received)
    return [lax.dynamic_index_in_dim(stacked, (pos - q) % width, 0, keepdims=False) for q in range(width)]


def combine_over(peak, total, axis, digits):
    size = lax.axis_size(axis)
    packed = jnp.stack([peak, total])
    stride = 1
    for width in digits:
        parts = [packed] + [
            lax.ppermute(packed, axis, digit_partners(axis, size, stride, width, k)) for k in range(1, width)
        ]
        new_peak = parts[0][0]
        for part in parts[1:]:
            new_peak = jnp.maximum(new_peak, part[0])
        terms = [part[1] * jnp.exp(part[0] - new_peak) for part in parts]
        if width == 4:
            new_total = (terms[0] + terms[2]) + (terms[1] + terms[3])
        else:
            new_total = terms[0] + terms[1]
        packed = jnp.stack([new_peak, new_total])
        stride *= width
    return packed[0] + jnp.log(packed[1])


def radix_digits(size):
    digits = []
    while size > 1:
        width = 4 if size % 4 == 0 else 2
        digits.append(width)
        size //= width
    return tuple(digits)


def col_digits(size):
    if size % 2 == 0:
        return (2,) + radix_digits(size // 2)
    return radix_digits(size)


def logsum_col(gaps, scale):
    peak = jnp.max(gaps, axis=1) / scale
    totals = jnp.sum(jnp.exp(gaps / scale - peak[:, None]), axis=1)
    return combine_over(peak, totals, "col", col_digits(lax.axis_size("col")))


def logsum_row(gaps, scale):
    peak = jnp.max(gaps, axis=0) / scale
    totals = jnp.sum(jnp.exp(gaps / scale - peak[None, :]), axis=0)
    return combine_over(peak, totals, "row", radix_digits(lax.axis_size("row")))


def gather_col(x):
    size = lax.axis_size("col")
    return jnp.concatenate(exchange(x, "col", 1, size), axis=0)


def gather_row(x):
    stride = 1
    for width in radix_digits(lax.axis_size("row")):
        x = jnp.concatenate(exchange(x, "row", stride, width), axis=0)
        stride *= width
    return x


def per_device(queries, passages, mean_cost):
    entropy_scale = 0.1 * mean_cost[0]
    row_count = lax.axis_size("row")
    col_count = lax.axis_size("col")
    all_queries = queries.shape[0] * row_count * col_count
    all_passages = passages.shape[0] * row_count * col_count
    query_block = gather_col(queries)
    half = passages.shape[1] // 2
    passage_block = jnp.concatenate(
        [lax.all_gather(passages[:, :half], "row", axis=0, tiled=True), gather_row(passages[:, half:])], axis=1
    )
    cost_tile = inner_costs(query_block, passage_block)
    col_potential = jnp.zeros((cost_tile.shape[1],), jnp.float32)
    row_potential = jnp.zeros((cost_tile.shape[0],), jnp.float32)
    for repeat in range(ITERS):
        gaps = col_potential[None, :] - cost_tile
        row_potential = -entropy_scale * math.log(all_queries) - entropy_scale * logsum_col(gaps, entropy_scale)
        gaps = row_potential[:, None] - cost_tile
        col_potential = -entropy_scale * math.log(all_passages) - entropy_scale * logsum_row(gaps, entropy_scale)
    return (row_potential, col_potential)


def solution(mesh):
    placed = (P(("row", "col"), None), P(("col", "row"), None), P())
    return jax.shard_map(
        per_device, mesh=mesh, in_specs=placed, out_specs=(P("row"), P("col")), check_vma=False
    )
```

```python
import math

import jax
import jax.numpy as jnp
from jax import lax
from jax.sharding import PartitionSpec as P

ITERS = 3


def inner_costs(left, right):
    left_norms = jnp.sum(left * left, axis=1)
    right_norms = jnp.sum(right * right, axis=1)
    inner = lax.dot_general(
        left,
        right,
        (((1,), (1,)), ((), ())),
        precision=lax.Precision.HIGHEST,
        preferred_element_type=jnp.float32,
    )
    return left_norms[:, None] + right_norms[None, :] - 2.0 * inner


def digit_partners(axis, size, stride, width, shift):
    perm = []
    for i in range(size):
        p = (i // stride) % width
        perm.append((i, i + (((p + shift) % width) - p) * stride))
    return perm


def exchange(x, axis, stride, width):
    size = lax.axis_size(axis)
    pos = (lax.axis_index(axis) // stride) % width
    received = [x] + [lax.ppermute(x, axis, digit_partners(axis, size, stride, width, k)) for k in range(1, width)]
    stacked = jnp.stack(received)
    return [lax.dynamic_index_in_dim(stacked, (pos - q) % width, 0, keepdims=False) for q in range(width)]


def combine_over(peak, total, axis, digits):
    size = lax.axis_size(axis)
    packed = jnp.stack([peak, total])
    stride = 1
    for width in digits:
        parts = [packed] + [
            lax.ppermute(packed, axis, digit_partners(axis, size, stride, width, k)) for k in range(1, width)
        ]
        new_peak = parts[0][0]
        for part in parts[1:]:
            new_peak = jnp.maximum(new_peak, part[0])
        terms = [part[1] * jnp.exp(part[0] - new_peak) for part in parts]
        if width == 4:
            new_total = (terms[0] + terms[2]) + (terms[1] + terms[3])
        else:
            new_total = terms[0] + terms[1]
        packed = jnp.stack([new_peak, new_total])
        stride *= width
    return packed[0] + jnp.log(packed[1])


def radix_digits(size):
    digits = []
    while size > 1:
        width = 4 if size % 4 == 0 else 2
        digits.append(width)
        size //= width
    return tuple(digits)


def col_digits(size):
    if size % 2 == 0:
        return (2,) + radix_digits(size // 2)
    return radix_digits(size)


def logsum_col(gaps, scale):
    peak = jnp.max(gaps, axis=1) / scale
    totals = jnp.sum(jnp.exp(gaps / scale - peak[:, None]), axis=1)
    return combine_over(peak, totals, "col", col_digits(lax.axis_size("col")))


def logsum_row(gaps, scale):
    peak = jnp.max(gaps, axis=0) / scale
    totals = jnp.sum(jnp.exp(gaps / scale - peak[None, :]), axis=0)
    return combine_over(peak, totals, "row", radix_digits(lax.axis_size("row")))


def gather_col(x):
    size = lax.axis_size("col")
    return jnp.concatenate(exchange(x, "col", 1, size), axis=0)


def gather_row(x):
    stride = 1
    for width in radix_digits(lax.axis_size("row")):
        x = jnp.concatenate(exchange(x, "row", stride, width), axis=0)
        stride *= width
    return x


def per_device(queries, passages, mean_cost):
    entropy_scale = 0.1 * mean_cost[0]
    row_count = lax.axis_size("row")
    col_count = lax.axis_size("col")
    all_queries = queries.shape[0] * row_count * col_count
    all_passages = passages.shape[0] * row_count * col_count
    query_block = gather_col(queries)
    rows = passages.shape[0]
    split = rows - rows // 4
    passage_block = jnp.concatenate(
        [lax.all_gather(passages[:split], "row", axis=0, tiled=True), gather_row(passages[split:])], axis=0
    )
    cost_tile = inner_costs(query_block, passage_block)
    col_potential = jnp.zeros((cost_tile.shape[1],), jnp.float32)
    row_potential = jnp.zeros((cost_tile.shape[0],), jnp.float32)
    for repeat in range(ITERS):
        gaps = col_potential[None, :] - cost_tile
        row_potential = -entropy_scale * math.log(all_queries) - entropy_scale * logsum_col(gaps, entropy_scale)
        gaps = row_potential[:, None] - cost_tile
        col_potential = -entropy_scale * math.log(all_passages) - entropy_scale * logsum_row(gaps, entropy_scale)
    head = col_potential[: split * row_count].reshape(row_count, split)
    tail = col_potential[split * row_count :].reshape(row_count, rows - split)
    return (row_potential, jnp.concatenate([head, tail], axis=1).reshape(-1))


def solution(mesh):
    placed = (P(("row", "col"), None), P(("col", "row"), None), P())
    return jax.shard_map(
        per_device, mesh=mesh, in_specs=placed, out_specs=(P("row"), P("col")), check_vma=False
    )
```

```python
import math

import jax
import jax.numpy as jnp
from jax import lax
from jax.sharding import PartitionSpec as P

ITERS = 3


def inner_costs(left, right):
    left_norms = jnp.sum(left * left, axis=1)
    right_norms = jnp.sum(right * right, axis=1)
    inner = lax.dot_general(
        left,
        right,
        (((1,), (1,)), ((), ())),
        precision=lax.Precision.HIGHEST,
        preferred_element_type=jnp.float32,
    )
    return left_norms[:, None] + right_norms[None, :] - 2.0 * inner


def digit_partners(axis, size, stride, width, shift):
    perm = []
    for i in range(size):
        p = (i // stride) % width
        perm.append((i, i + (((p + shift) % width) - p) * stride))
    return perm


def exchange(x, axis, stride, width):
    size = lax.axis_size(axis)
    pos = (lax.axis_index(axis) // stride) % width
    received = [x] + [lax.ppermute(x, axis, digit_partners(axis, size, stride, width, k)) for k in range(1, width)]
    stacked = jnp.stack(received)
    return [lax.dynamic_index_in_dim(stacked, (pos - q) % width, 0, keepdims=False) for q in range(width)]


def combine_over(peak, total, axis, digits):
    size = lax.axis_size(axis)
    packed = jnp.stack([peak, total])
    stride = 1
    for width in digits:
        parts = [packed] + [
            lax.ppermute(packed, axis, digit_partners(axis, size, stride, width, k)) for k in range(1, width)
        ]
        new_peak = parts[0][0]
        for part in parts[1:]:
            new_peak = jnp.maximum(new_peak, part[0])
        terms = [part[1] * jnp.exp(part[0] - new_peak) for part in parts]
        if width == 4:
            new_total = (terms[0] + terms[2]) + (terms[1] + terms[3])
        else:
            new_total = terms[0] + terms[1]
        packed = jnp.stack([new_peak, new_total])
        stride *= width
    return packed[0] + jnp.log(packed[1])


def radix_digits(size):
    digits = []
    while size > 1:
        width = 4 if size % 4 == 0 else 2
        digits.append(width)
        size //= width
    return tuple(digits)


def col_digits(size):
    if size % 2 == 0:
        return (2,) + radix_digits(size // 2)
    return radix_digits(size)


def logsum_col(gaps, scale):
    peak = jnp.max(gaps, axis=1) / scale
    totals = jnp.sum(jnp.exp(gaps / scale - peak[:, None]), axis=1)
    return combine_over(peak, totals, "col", col_digits(lax.axis_size("col")))


def logsum_row(gaps, scale):
    peak = jnp.max(gaps, axis=0) / scale
    totals = jnp.sum(jnp.exp(gaps / scale - peak[None, :]), axis=0)
    return combine_over(peak, totals, "row", radix_digits(lax.axis_size("row")))


def gather_col(x):
    size = lax.axis_size("col")
    return jnp.concatenate(exchange(x, "col", 1, size), axis=0)


def gather_row(x):
    stride = 1
    for width in radix_digits(lax.axis_size("row")):
        x = jnp.concatenate(exchange(x, "row", stride, width), axis=0)
        stride *= width
    return x


def per_device(queries, passages, mean_cost):
    entropy_scale = 0.1 * mean_cost[0]
    row_count = lax.axis_size("row")
    col_count = lax.axis_size("col")
    all_queries = queries.shape[0] * row_count * col_count
    all_passages = passages.shape[0] * row_count * col_count
    query_block = gather_col(queries)
    rows = passages.shape[0]
    split = rows - rows // 8
    passage_block = jnp.concatenate(
        [lax.all_gather(passages[:split], "row", axis=0, tiled=True), gather_row(passages[split:])], axis=0
    )
    cost_tile = inner_costs(query_block, passage_block)
    col_potential = jnp.zeros((cost_tile.shape[1],), jnp.float32)
    row_potential = jnp.zeros((cost_tile.shape[0],), jnp.float32)
    for repeat in range(ITERS):
        gaps = col_potential[None, :] - cost_tile
        row_potential = -entropy_scale * math.log(all_queries) - entropy_scale * logsum_col(gaps, entropy_scale)
        gaps = row_potential[:, None] - cost_tile
        col_potential = -entropy_scale * math.log(all_passages) - entropy_scale * logsum_row(gaps, entropy_scale)
    head = col_potential[: split * row_count].reshape(row_count, split)
    tail = col_potential[split * row_count :].reshape(row_count, rows - split)
    return (row_potential, jnp.concatenate([head, tail], axis=1).reshape(-1))


def solution(mesh):
    placed = (P(("row", "col"), None), P(("col", "row"), None), P())
    return jax.shard_map(
        per_device, mesh=mesh, in_specs=placed, out_specs=(P("row"), P("col")), check_vma=False
    )
```

```python
import math

import jax
import jax.numpy as jnp
from jax import lax
from jax.sharding import PartitionSpec as P

ITERS = 3


def inner_costs(left, right):
    left_norms = jnp.sum(left * left, axis=1)
    right_norms = jnp.sum(right * right, axis=1)
    inner = lax.dot_general(
        left,
        right,
        (((1,), (1,)), ((), ())),
        precision=lax.Precision.HIGHEST,
        preferred_element_type=jnp.float32,
    )
    return left_norms[:, None] + right_norms[None, :] - 2.0 * inner


def digit_partners(axis, size, stride, width, shift):
    perm = []
    for i in range(size):
        p = (i // stride) % width
        perm.append((i, i + (((p + shift) % width) - p) * stride))
    return perm


def exchange(x, axis, stride, width):
    size = lax.axis_size(axis)
    pos = (lax.axis_index(axis) // stride) % width
    received = [x] + [lax.ppermute(x, axis, digit_partners(axis, size, stride, width, k)) for k in range(1, width)]
    stacked = jnp.stack(received)
    return [lax.dynamic_index_in_dim(stacked, (pos - q) % width, 0, keepdims=False) for q in range(width)]


def combine_over(peak, total, axis, digits):
    size = lax.axis_size(axis)
    packed = jnp.stack([peak, total])
    stride = 1
    for width in digits:
        parts = [packed] + [
            lax.ppermute(packed, axis, digit_partners(axis, size, stride, width, k)) for k in range(1, width)
        ]
        new_peak = parts[0][0]
        for part in parts[1:]:
            new_peak = jnp.maximum(new_peak, part[0])
        terms = [part[1] * jnp.exp(part[0] - new_peak) for part in parts]
        if width == 4:
            new_total = (terms[0] + terms[2]) + (terms[1] + terms[3])
        else:
            new_total = terms[0] + terms[1]
        packed = jnp.stack([new_peak, new_total])
        stride *= width
    return packed[0] + jnp.log(packed[1])


def radix_digits(size):
    digits = []
    while size > 1:
        width = 4 if size % 4 == 0 else 2
        digits.append(width)
        size //= width
    return tuple(digits)


def col_digits(size):
    if size % 2 == 0:
        return (2,) + radix_digits(size // 2)
    return radix_digits(size)


def logsum_col(gaps, scale):
    peak = jnp.max(gaps, axis=1) / scale
    totals = jnp.sum(jnp.exp(gaps / scale - peak[:, None]), axis=1)
    return combine_over(peak, totals, "col", col_digits(lax.axis_size("col")))


def logsum_row(gaps, scale):
    peak = jnp.max(gaps, axis=0) / scale
    totals = jnp.sum(jnp.exp(gaps / scale - peak[None, :]), axis=0)
    return combine_over(peak, totals, "row", radix_digits(lax.axis_size("row")))


def gather_col(x):
    size = lax.axis_size("col")
    return jnp.concatenate(exchange(x, "col", 1, size), axis=0)


def gather_row(x):
    stride = 1
    for width in radix_digits(lax.axis_size("row")):
        x = jnp.concatenate(exchange(x, "row", stride, width), axis=0)
        stride *= width
    return x


def per_device(queries, passages, mean_cost):
    entropy_scale = 0.1 * mean_cost[0]
    row_count = lax.axis_size("row")
    col_count = lax.axis_size("col")
    all_queries = queries.shape[0] * row_count * col_count
    all_passages = passages.shape[0] * row_count * col_count
    query_block = gather_col(queries)
    rows = passages.shape[0]
    split = rows - rows // 16
    passage_block = jnp.concatenate(
        [lax.all_gather(passages[:split], "row", axis=0, tiled=True), gather_row(passages[split:])], axis=0
    )
    cost_tile = inner_costs(query_block, passage_block)
    col_potential = jnp.zeros((cost_tile.shape[1],), jnp.float32)
    row_potential = jnp.zeros((cost_tile.shape[0],), jnp.float32)
    for repeat in range(ITERS):
        gaps = col_potential[None, :] - cost_tile
        row_potential = -entropy_scale * math.log(all_queries) - entropy_scale * logsum_col(gaps, entropy_scale)
        gaps = row_potential[:, None] - cost_tile
        col_potential = -entropy_scale * math.log(all_passages) - entropy_scale * logsum_row(gaps, entropy_scale)
    head = col_potential[: split * row_count].reshape(row_count, split)
    tail = col_potential[split * row_count :].reshape(row_count, rows - split)
    return (row_potential, jnp.concatenate([head, tail], axis=1).reshape(-1))


def solution(mesh):
    placed = (P(("row", "col"), None), P(("col", "row"), None), P())
    return jax.shard_map(
        per_device, mesh=mesh, in_specs=placed, out_specs=(P("row"), P("col")), check_vma=False
    )
```

```python
import math

import jax
import jax.numpy as jnp
from jax import lax
from jax.sharding import PartitionSpec as P

ITERS = 3


def inner_costs(left, right):
    left_norms = jnp.sum(left * left, axis=1)
    right_norms = jnp.sum(right * right, axis=1)
    inner = lax.dot_general(
        left,
        right,
        (((1,), (1,)), ((), ())),
        precision=lax.Precision.HIGHEST,
        preferred_element_type=jnp.float32,
    )
    return left_norms[:, None] + right_norms[None, :] - 2.0 * inner


def digit_partners(axis, size, stride, width, shift):
    perm = []
    for i in range(size):
        p = (i // stride) % width
        perm.append((i, i + (((p + shift) % width) - p) * stride))
    return perm


def exchange(x, axis, stride, width):
    size = lax.axis_size(axis)
    pos = (lax.axis_index(axis) // stride) % width
    received = [x] + [lax.ppermute(x, axis, digit_partners(axis, size, stride, width, k)) for k in range(1, width)]
    stacked = jnp.stack(received)
    return [lax.dynamic_index_in_dim(stacked, (pos - q) % width, 0, keepdims=False) for q in range(width)]


def combine_over(peak, total, axis, digits):
    size = lax.axis_size(axis)
    packed = jnp.stack([peak, total])
    stride = 1
    for width in digits:
        parts = [packed] + [
            lax.ppermute(packed, axis, digit_partners(axis, size, stride, width, k)) for k in range(1, width)
        ]
        new_peak = parts[0][0]
        for part in parts[1:]:
            new_peak = jnp.maximum(new_peak, part[0])
        terms = [part[1] * jnp.exp(part[0] - new_peak) for part in parts]
        if width == 4:
            new_total = (terms[0] + terms[2]) + (terms[1] + terms[3])
        else:
            new_total = terms[0] + terms[1]
        packed = jnp.stack([new_peak, new_total])
        stride *= width
    return packed[0] + jnp.log(packed[1])


def radix_digits(size):
    digits = []
    while size > 1:
        width = 4 if size % 4 == 0 else 2
        digits.append(width)
        size //= width
    return tuple(digits)


def col_digits(size):
    if size % 2 == 0:
        return (2,) + radix_digits(size // 2)
    return radix_digits(size)


def logsum_col(gaps, scale):
    peak = jnp.max(gaps, axis=1) / scale
    totals = jnp.sum(jnp.exp(gaps / scale - peak[:, None]), axis=1)
    return combine_over(peak, totals, "col", col_digits(lax.axis_size("col")))


def logsum_row(gaps, scale):
    peak = jnp.max(gaps, axis=0) / scale
    totals = jnp.sum(jnp.exp(gaps / scale - peak[None, :]), axis=0)
    return combine_over(peak, totals, "row", radix_digits(lax.axis_size("row")))


def gather_col(x):
    size = lax.axis_size("col")
    return jnp.concatenate(exchange(x, "col", 1, size), axis=0)


def gather_row(x):
    stride = 1
    for width in radix_digits(lax.axis_size("row")):
        x = jnp.concatenate(exchange(x, "row", stride, width), axis=0)
        stride *= width
    return x


def per_device(queries, passages, mean_cost):
    entropy_scale = 0.1 * mean_cost[0]
    row_count = lax.axis_size("row")
    col_count = lax.axis_size("col")
    all_queries = queries.shape[0] * row_count * col_count
    all_passages = passages.shape[0] * row_count * col_count
    query_block = gather_col(queries)
    rows = passages.shape[0]
    split = rows - (rows * 3) // 32
    passage_block = jnp.concatenate(
        [lax.all_gather(passages[:split], "row", axis=0, tiled=True), gather_row(passages[split:])], axis=0
    )
    cost_tile = inner_costs(query_block, passage_block)
    col_potential = jnp.zeros((cost_tile.shape[1],), jnp.float32)
    row_potential = jnp.zeros((cost_tile.shape[0],), jnp.float32)
    for repeat in range(ITERS):
        gaps = col_potential[None, :] - cost_tile
        row_potential = -entropy_scale * math.log(all_queries) - entropy_scale * logsum_col(gaps, entropy_scale)
        gaps = row_potential[:, None] - cost_tile
        col_potential = -entropy_scale * math.log(all_passages) - entropy_scale * logsum_row(gaps, entropy_scale)
    head = col_potential[: split * row_count].reshape(row_count, split)
    tail = col_potential[split * row_count :].reshape(row_count, rows - split)
    return (row_potential, jnp.concatenate([head, tail], axis=1).reshape(-1))


def solution(mesh):
    placed = (P(("row", "col"), None), P(("col", "row"), None), P())
    return jax.shard_map(
        per_device, mesh=mesh, in_specs=placed, out_specs=(P("row"), P("col")), check_vma=False
    )
```

```python
import math

import jax
import jax.numpy as jnp
from jax import lax
from jax.sharding import PartitionSpec as P

ITERS = 3


def inner_costs(left, right):
    left_norms = jnp.sum(left * left, axis=1)
    right_norms = jnp.sum(right * right, axis=1)
    inner = lax.dot_general(
        left,
        right,
        (((1,), (1,)), ((), ())),
        precision=lax.Precision.HIGHEST,
        preferred_element_type=jnp.float32,
    )
    return left_norms[:, None] + right_norms[None, :] - 2.0 * inner


def digit_partners(axis, size, stride, width, shift):
    perm = []
    for i in range(size):
        p = (i // stride) % width
        perm.append((i, i + (((p + shift) % width) - p) * stride))
    return perm


def exchange(x, axis, stride, width):
    size = lax.axis_size(axis)
    pos = (lax.axis_index(axis) // stride) % width
    received = [x] + [lax.ppermute(x, axis, digit_partners(axis, size, stride, width, k)) for k in range(1, width)]
    stacked = jnp.stack(received)
    return [lax.dynamic_index_in_dim(stacked, (pos - q) % width, 0, keepdims=False) for q in range(width)]


def combine_over(peak, total, axis, digits):
    size = lax.axis_size(axis)
    packed = jnp.stack([peak, total])
    stride = 1
    for width in digits:
        parts = [packed] + [
            lax.ppermute(packed, axis, digit_partners(axis, size, stride, width, k)) for k in range(1, width)
        ]
        new_peak = parts[0][0]
        for part in parts[1:]:
            new_peak = jnp.maximum(new_peak, part[0])
        terms = [part[1] * jnp.exp(part[0] - new_peak) for part in parts]
        if width == 4:
            new_total = (terms[0] + terms[2]) + (terms[1] + terms[3])
        else:
            new_total = terms[0] + terms[1]
        packed = jnp.stack([new_peak, new_total])
        stride *= width
    return packed[0] + jnp.log(packed[1])


def radix_digits(size):
    digits = []
    while size > 1:
        width = 4 if size % 4 == 0 else 2
        digits.append(width)
        size //= width
    return tuple(digits)


def col_digits(size):
    if size % 2 == 0:
        return (2,) + radix_digits(size // 2)
    return radix_digits(size)


def logsum_col(gaps, scale):
    peak = jnp.max(gaps, axis=1) / scale
    totals = jnp.sum(jnp.exp(gaps / scale - peak[:, None]), axis=1)
    return combine_over(peak, totals, "col", col_digits(lax.axis_size("col")))


def logsum_row(gaps, scale):
    peak = jnp.max(gaps, axis=0) / scale
    totals = jnp.sum(jnp.exp(gaps / scale - peak[None, :]), axis=0)
    return combine_over(peak, totals, "row", radix_digits(lax.axis_size("row")))


def gather_col(x):
    size = lax.axis_size("col")
    return jnp.concatenate(exchange(x, "col", 1, size), axis=0)


def gather_row(x):
    stride = 1
    for width in radix_digits(lax.axis_size("row")):
        x = jnp.concatenate(exchange(x, "row", stride, width), axis=0)
        stride *= width
    return x


def per_device(queries, passages, mean_cost):
    entropy_scale = 0.1 * mean_cost[0]
    row_count = lax.axis_size("row")
    col_count = lax.axis_size("col")
    all_queries = queries.shape[0] * row_count * col_count
    all_passages = passages.shape[0] * row_count * col_count
    query_block = gather_col(queries)
    rows = passages.shape[0]
    split = rows - (rows * 5) // 32
    passage_block = jnp.concatenate(
        [lax.all_gather(passages[:split], "row", axis=0, tiled=True), gather_row(passages[split:])], axis=0
    )
    cost_tile = inner_costs(query_block, passage_block)
    col_potential = jnp.zeros((cost_tile.shape[1],), jnp.float32)
    row_potential = jnp.zeros((cost_tile.shape[0],), jnp.float32)
    for repeat in range(ITERS):
        gaps = col_potential[None, :] - cost_tile
        row_potential = -entropy_scale * math.log(all_queries) - entropy_scale * logsum_col(gaps, entropy_scale)
        gaps = row_potential[:, None] - cost_tile
        col_potential = -entropy_scale * math.log(all_passages) - entropy_scale * logsum_row(gaps, entropy_scale)
    head = col_potential[: split * row_count].reshape(row_count, split)
    tail = col_potential[split * row_count :].reshape(row_count, rows - split)
    return (row_potential, jnp.concatenate([head, tail], axis=1).reshape(-1))


def solution(mesh):
    placed = (P(("row", "col"), None), P(("col", "row"), None), P())
    return jax.shard_map(
        per_device, mesh=mesh, in_specs=placed, out_specs=(P("row"), P("col")), check_vma=False
    )
```
